32 devices in a mesh: row: 4 (over z), col: 4 (over y, x), seq: 2 (over core).
Axes of the slice: x: 2, y: 2, z: 4, core: 2. Of those that a mesh axis runs over, the one named last changes fastest.
Arguments:
- tokens: bfloat16 [32, 12288], P(('col', 'seq'), 'row'), may hold values from -6 to 6
- cotangent: bfloat16 [32, 12288], P(('col', 'seq'), 'row'), may hold values from -6 to 6
- up_values: bfloat16 [4, 8, 576, 128, 128], P('row', ('col', 'seq')), may hold values from -0.109375 to 0.109375
- up_index: int32 [4, 8, 576], P('row', ('col', 'seq')), may hold values from 0 to 1151, as said below
- up_count: int32 [4, 8], P('row', ('col', 'seq')), may hold values from 144 to 576, as said below
- down_values: bfloat16 [4, 8, 576, 128, 128], P('row', ('col', 'seq')), may hold values from -0.0546875 to 0.0546875
- down_index: int32 [4, 8, 576], P('row', ('col', 'seq')), may hold values from 0 to 1151, as said below
- down_count: int32 [4, 8], P('row', ('col', 'seq')), may hold values from 144 to 576, as said below
Outputs:
- output: bfloat16 [32, 12288], P(('col', 'seq'), 'row')
- grad_tokens: bfloat16 [32, 12288], P(('col', 'seq'), 'row')
The draws below stay inside these ranges and needn't reach their ends.
Inputs may be any that keep to these rules, and one draw needn't show every extreme that they name: `up_index`: in every tile, the slots below its count hold distinct block numbers, block row within the tile times 48 plus block column; later slots hold block numbers too and are unused. `down_index`: in every tile, the slots below its count hold distinct block numbers, block row along the model width times 48 plus block column along the hidden units; later slots hold block numbers too and are unused. `up_count`: some tile has exactly 576 nonzero blocks. `down_count`: some tile has exactly 576 nonzero blocks.
All inputs are finite; a program needn't handle non-finite values.
Results may differ from the reference program's by a relative error of at most 0.0049.
Values may be sent and summed in bfloat16 or wider, within the bound.
No kernel may reach another device: no remote copies, remote signals or barrier semaphores. Data moves between devices by JAX's collectives and lax.ppermute only.
A program may use at most 128 MiB of HBM per device.

```python
import jax
import jax.numpy as jnp
from jax import lax

D = 12288
FF = 49152
BLK = 128
TOKENS = 32
ROWT = 4
COLT = 8
BR = 24
BC = 48
NBLK = 1152
MAXNZ = 576
N_ROW = 4
N_COL = 4
N_SEQ = 2


def draw_counts(key):
    tile_total = N_ROW * N_COL * N_SEQ
    fewest = NBLK // 8
    ticket = jax.random.randint(jax.random.fold_in(key, 1), (tile_total,), 0, 1024)
    counts = fewest + ticket * ticket * (MAXNZ - fewest) // (1024 * 1024)
    busiest = jax.random.randint(jax.random.fold_in(key, 2), (), 0, tile_total)
    counts = jnp.where(jnp.arange(tile_total) == busiest, MAXNZ, counts)
    return counts.reshape(N_ROW, N_COL * N_SEQ).astype(jnp.int32)


def draw_indices(key):
    tile_total = N_ROW * N_COL * N_SEQ
    tile_keys = jax.random.split(key, tile_total)
    orders = jax.vmap(lambda single: jax.random.permutation(single, NBLK))(tile_keys)
    return orders[:, :MAXNZ].reshape(N_ROW, N_COL * N_SEQ, MAXNZ).astype(jnp.int32)


def draw_up_count(key, part):
    return draw_counts(jax.random.fold_in(key, 11))


def draw_down_count(key, part):
    return draw_counts(jax.random.fold_in(key, 22))


def draw_up_index(key, part):
    return draw_indices(jax.random.fold_in(key, 33))


def draw_down_index(key, part):
    return draw_indices(jax.random.fold_in(key, 44))


def levels(own_key, extent, pieces, smallest, largest):
    loudness = 1.0
    for position, shards_of in pieces:
        heights = jax.random.uniform(jax.random.fold_in(jax.random.fold_in(own_key, 6), position), (shards_of,), jnp.float32, smallest / len(pieces), largest / len(pieces))
        loudness = loudness * jnp.repeat(jnp.exp(heights), extent[position] // shards_of).reshape((-1,) + (1,) * (len(extent) - 1 - position))
    return loudness


def normal_values(stream_key, shape, width, limit, shards=(), kind=jnp.bfloat16):
    drawn = width * jax.random.normal(stream_key, shape, jnp.float32)
    if shards:
        drawn = drawn * levels(stream_key, shape, shards, -0.22, 0.18)
    return jnp.clip(drawn, -limit, limit).astype(kind)


def setup_inputs(seed: int = 0) -> dict:
    splits = jax.random.split(jax.random.key(seed), 9)
    return {
        "tokens": normal_values(splits[0], (TOKENS, D), 1.0, 6.0, ((0, 8), (1, 4))),
        "cotangent": normal_values(splits[1], (TOKENS, D), 1.0, 6.0, ((0, 8), (1, 4))),
        "up_values": normal_values(splits[2], (ROWT, COLT, MAXNZ, BLK, BLK), (D // 4) ** -0.5, 0.109375, ((0, 4), (1, 8))),
        "up_index": draw_up_index(jax.random.fold_in(splits[8], 71), 0),
        "up_count": draw_up_count(jax.random.fold_in(splits[8], 71), 0),
        "down_values": normal_values(splits[5], (ROWT, COLT, MAXNZ, BLK, BLK), (FF // 4) ** -0.5, 0.0546875, ((0, 4), (1, 8))),
        "down_index": draw_down_index(jax.random.fold_in(splits[8], 71), 0),
        "down_count": draw_down_count(jax.random.fold_in(splits[8], 71), 0),
    }


def gelu_forward(inputs):
    return jax.nn.gelu(inputs, approximate=True)

def gelu_backward(pre_act, gradient):
    return jax.vjp(gelu_forward, pre_act)[1](gradient)[0]

def block_product(inputs, values, pick_index, put_index, live_mask, out_blocks, flipped):
    count_rows = inputs.shape[0]
    block_size = values.shape[-1]
    blocks = inputs.reshape(count_rows, -1, block_size)
    picked = jnp.take(blocks, pick_index, axis=1).astype(jnp.float32)
    weights = values.astype(jnp.float32)
    pattern = 'tkc,koc->tko' if flipped else 'tkc,kco->tko'
    product = jnp.einsum(pattern, picked, weights, precision=lax.Precision.HIGHEST)
    placing = ((put_index[:, None] == jnp.arange(out_blocks, dtype=jnp.int32)[None, :]) & live_mask[:, None]).astype(jnp.float32)
    placed = jnp.einsum('tko,kn->tno', product, placing, precision=lax.Precision.HIGHEST)
    return placed.reshape(count_rows, out_blocks * block_size)

def reference(tokens, cotangent, up_values, up_index, up_count, down_values, down_index, down_count):
    tile_rows = D // ROWT
    tile_cols = FF // COLT
    count_rows = tokens.shape[0]
    slot_ids = jnp.arange(MAXNZ, dtype=jnp.int32)

    def tile_layout(index, counts, row_id, col_id):
        chosen = index[row_id, col_id]
        return (chosen // BC, chosen % BC, slot_ids < counts[row_id, col_id])

    def column_pass(col_id):

        def add_row(carry, row_id):
            offset = (row_id * tile_rows).astype(jnp.int32)
            tok_part = lax.dynamic_slice_in_dim(tokens, offset, tile_rows, 1)
            cot_part = lax.dynamic_slice_in_dim(cotangent, offset, tile_rows, 1)
            up_rowblk, up_colblk, up_live = tile_layout(up_index, up_count, row_id, col_id)
            down_rowblk, down_colblk, down_live = tile_layout(down_index, down_count, row_id, col_id)
            pre_part = block_product(tok_part, up_values[row_id, col_id], up_rowblk, up_colblk, up_live, BC, False)
            grad_part = block_product(cot_part, down_values[row_id, col_id], down_rowblk, down_colblk, down_live, BC, True)
            return ((carry[0] + pre_part, carry[1] + grad_part), None)
        zeros = jnp.zeros((count_rows, tile_cols), jnp.float32)
        (pre_act, grad_act), _ = lax.scan(add_row, (zeros, zeros), jnp.arange(ROWT, dtype=jnp.int32))
        return (gelu_forward(pre_act).astype(jnp.bfloat16), gelu_backward(pre_act, grad_act).astype(jnp.bfloat16))
    activation, grad_pre = lax.map(column_pass, jnp.arange(COLT, dtype=jnp.int32))

    def row_pass(row_id):

        def add_column(carry, col_id):
            up_rowblk, up_colblk, up_live = tile_layout(up_index, up_count, row_id, col_id)
            down_rowblk, down_colblk, down_live = tile_layout(down_index, down_count, row_id, col_id)
            out_part = block_product(activation[col_id], down_values[row_id, col_id], down_colblk, down_rowblk, down_live, BR, False)
            back_part = block_product(grad_pre[col_id], up_values[row_id, col_id], up_colblk, up_rowblk, up_live, BR, True)
            return ((carry[0] + out_part, carry[1] + back_part), None)
        zeros = jnp.zeros((count_rows, tile_rows), jnp.float32)
        sums, _ = lax.scan(add_column, (zeros, zeros), jnp.arange(COLT, dtype=jnp.int32))
        return sums
    outputs, backs = lax.map(row_pass, jnp.arange(ROWT, dtype=jnp.int32))
    output = jnp.transpose(outputs, (1, 0, 2)).reshape(count_rows, D).astype(jnp.bfloat16)
    grad_tokens = jnp.transpose(backs, (1, 0, 2)).reshape(count_rows, D).astype(jnp.bfloat16)
    return (output, grad_tokens)
```

```python
import jax
import jax.numpy as jnp
from jax import lax
from jax.experimental import pallas as pl
from jax.experimental.pallas import tpu as pltpu
from jax.sharding import PartitionSpec as P

FF = 49152


def gelu_forward(inputs):
    return jax.nn.gelu(inputs, approximate=True)


def gelu_backward(pre_act, gradient):
    return jax.vjp(gelu_forward, pre_act)[1](gradient)[0]


def activate(paired):
    pre_act = paired[0]
    return jnp.stack(
        [
            gelu_forward(pre_act).astype(jnp.bfloat16),
            gelu_backward(pre_act, paired[1]).astype(jnp.bfloat16),
        ]
    )


def group_size(slots):
    best = 1
    for size in range(1, 33):
        if slots % size == 0:
            best = size
    return best


def block_kernel(group, flips):
    def kernel(pick0, put0, pick1, put1, counts, x0, x1, w0, w1, o0, o1):
        step = pl.program_id(0)

        @pl.when(step == 0)
        def _():
            o0[...] = jnp.zeros_like(o0)
            o1[...] = jnp.zeros_like(o1)

        streams = ((pick0, put0, x0, w0, o0, flips[0], 0), (pick1, put1, x1, w1, o1, flips[1], 1))
        for pick, put, x, w, o, flipped, which in streams:
            live = counts[which]

            def body(j, carry, pick=pick, put=put, x=x, w=w, o=o, flipped=flipped, live=live):
                slot = step * group + j

                @pl.when(slot < live)
                def _():
                    src = x[pick[slot]]
                    blk = w[j]
                    if flipped:
                        prod = lax.dot_general(
                            src, blk, (((1,), (1,)), ((), ())),
                            preferred_element_type=jnp.float32,
                        )
                    else:
                        prod = jnp.dot(src, blk, preferred_element_type=jnp.float32)
                    dst = put[slot]
                    o[dst] = o[dst] + prod

                return carry

            lax.fori_loop(0, group, body, 0, unroll=8)

    return kernel


def block_pass(x0, w0, pick0, put0, n0, x1, w1, pick1, put1, n1, out_blocks, flips):
    slots, blk, _ = w0.shape
    rows = x0.shape[1]
    group = group_size(slots)
    steps = slots // group
    counts = jnp.stack([n0, n1]).astype(jnp.int32)

    def w_map(which):
        def index_map(i, p0, q0, p1, q1, c):
            last = jnp.maximum(c[which] - 1, 0) // group
            return (jnp.minimum(i, last), 0, 0)

        return index_map

    def whole(shape):
        return pl.BlockSpec(shape, lambda i, p0, q0, p1, q1, c: (0, 0, 0))

    spec = pltpu.PrefetchScalarGridSpec(
        num_scalar_prefetch=5,
        grid=(steps,),
        in_specs=[
            whole(x0.shape),
            whole(x1.shape),
            pl.BlockSpec((group, blk, blk), w_map(0)),
            pl.BlockSpec((group, blk, blk), w_map(1)),
        ],
        out_specs=[
            whole((out_blocks, rows, blk)),
            whole((out_blocks, rows, blk)),
        ],
    )
    out_shape = [jax.ShapeDtypeStruct((out_blocks, rows, blk), jnp.float32)] * 2
    return pl.pallas_call(
        block_kernel(group, flips),
        grid_spec=spec,
        out_shape=out_shape,
        compiler_params=pltpu.CompilerParams(dimension_semantics=("arbitrary",)),
    )(pick0, put0, pick1, put1, counts, x0, x1, w0, w1)


def local(tokens, cotangent, up_values, up_index, up_count, down_values, down_index, down_count):
    block_size = up_values.shape[-1]
    tile_rows = tokens.shape[1]
    block_rows = tile_rows // block_size
    block_cols = FF // (block_size * lax.axis_size(("col", "seq")))
    up_vals = up_values[0, 0]
    up_chosen = up_index[0, 0]
    up_rowblk = up_chosen // block_cols
    up_colblk = up_chosen % block_cols
    down_vals = down_values[0, 0]
    down_chosen = down_index[0, 0]
    down_rowblk = down_chosen // block_cols
    down_colblk = down_chosen % block_cols
    up_n = up_count[0, 0]
    down_n = down_count[0, 0]

    stacked = jnp.stack([tokens, cotangent])
    local_rows = stacked.shape[1]
    blocked = stacked.reshape(2, local_rows, block_rows, block_size).transpose(0, 2, 1, 3)
    shard_rows = lax.all_gather(blocked, ("col", "seq"), axis=2, tiled=True)
    pre_part, grad_part = block_pass(
        shard_rows[0], up_vals, up_rowblk, up_colblk, up_n,
        shard_rows[1], down_vals, down_rowblk, down_colblk, down_n,
        block_cols, (False, True),
    )
    partial_value = jnp.stack([pre_part, grad_part])
    shares = lax.psum_scatter(partial_value, "row", scatter_dimension=2, tiled=True)
    activated = lax.all_gather(activate(shares), "row", axis=2, tiled=True)
    out_part, back_part = block_pass(
        activated[0], down_vals, down_colblk, down_rowblk, down_n,
        activated[1], up_vals, up_colblk, up_rowblk, up_n,
        block_rows, (False, True),
    )
    summed = lax.psum_scatter(
        jnp.stack([out_part, back_part]),
        ("col", "seq"),
        scatter_dimension=2,
        tiled=True,
    )
    result = summed.transpose(0, 2, 1, 3).reshape(2, local_rows, tile_rows).astype(jnp.bfloat16)
    return (result[0], result[1])


def solution(mesh):
    return jax.shard_map(
        local,
        mesh=mesh,
        in_specs=(
            P(("col", "seq"), "row"),
            P(("col", "seq"), "row"),
            P("row", ("col", "seq"), None, None, None),
            P("row", ("col", "seq"), None),
            P("row", ("col", "seq")),
            P("row", ("col", "seq"), None, None, None),
            P("row", ("col", "seq"), None),
            P("row", ("col", "seq")),
        ),
        out_specs=(P(("col", "seq"), "row"), P(("col", "seq"), "row")),
        check_vma=False,
    )
```

```python
import jax
import jax.numpy as jnp
from jax import lax
from jax.experimental import pallas as pl
from jax.experimental.pallas import tpu as pltpu
from jax.sharding import PartitionSpec as P

FF = 49152


def gelu_forward(inputs):
    return jax.nn.gelu(inputs, approximate=True)


def gelu_backward(pre_act, gradient):
    return jax.vjp(gelu_forward, pre_act)[1](gradient)[0]


def activate(paired):
    pre_act = paired[0]
    return jnp.stack(
        [
            gelu_forward(pre_act).astype(jnp.bfloat16),
            gelu_backward(pre_act, paired[1]).astype(jnp.bfloat16),
        ]
    )


def group_size(slots):
    best = 1
    for size in range(1, 97):
        if slots % size == 0:
            best = size
    return best


def block_kernel(group, flips):
    def kernel(pick0, put0, pick1, put1, counts, x0, x1, w0, w1, o0, o1):
        step = pl.program_id(0)
        first = step * group

        @pl.when(step == 0)
        def _():
            o0[...] = jnp.zeros_like(o0)
            o1[...] = jnp.zeros_like(o1)

        streams = ((pick0, put0, x0, w0, o0, flips[0], 0), (pick1, put1, x1, w1, o1, flips[1], 1))
        for pick, put, x, w, o, flipped, which in streams:
            live = counts[which]

            @pl.when(first < live)
            def _(pick=pick, put=put, x=x, w=w, o=o, flipped=flipped, live=live):
                for j in range(group):
                    slot = first + j
                    src = x[pick[slot]]
                    blk = w[j]
                    if flipped:
                        prod = lax.dot_general(
                            src, blk, (((1,), (1,)), ((), ())),
                            preferred_element_type=jnp.float32,
                        )
                    else:
                        prod = jnp.dot(src, blk, preferred_element_type=jnp.float32)
                    scale = jnp.where(slot < live, 1.0, 0.0).astype(jnp.float32)
                    dst = put[slot]
                    o[dst] = o[dst] + prod * scale

    return kernel


def block_pass(x0, w0, pick0, put0, n0, x1, w1, pick1, put1, n1, out_blocks, flips):
    slots, blk, _ = w0.shape
    rows = x0.shape[1]
    group = group_size(slots)
    steps = slots // group
    counts = jnp.stack([n0, n1]).astype(jnp.int32)

    def w_map(which):
        def index_map(i, p0, q0, p1, q1, c):
            last = jnp.maximum(c[which] - 1, 0) // group
            return (jnp.minimum(i, last), 0, 0)

        return index_map

    def whole(shape):
        return pl.BlockSpec(shape, lambda i, p0, q0, p1, q1, c: (0, 0, 0))

    spec = pltpu.PrefetchScalarGridSpec(
        num_scalar_prefetch=5,
        grid=(steps,),
        in_specs=[
            whole(x0.shape),
            whole(x1.shape),
            pl.BlockSpec((group, blk, blk), w_map(0)),
            pl.BlockSpec((group, blk, blk), w_map(1)),
        ],
        out_specs=[
            whole((out_blocks, rows, blk)),
            whole((out_blocks, rows, blk)),
        ],
    )
    out_shape = [jax.ShapeDtypeStruct((out_blocks, rows, blk), jnp.float32)] * 2
    return pl.pallas_call(
        block_kernel(group, flips),
        grid_spec=spec,
        out_shape=out_shape,
        compiler_params=pltpu.CompilerParams(dimension_semantics=("arbitrary",)),
    )(pick0, put0, pick1, put1, counts, x0, x1, w0, w1)


def exchange_sum(x, axis):
    count = lax.axis_size(axis)
    me = lax.axis_index(axis)
    chunks = x.reshape((count, x.shape[0] // count) + x.shape[1:])
    total = chunks[me]
    for shift in range(1, count):
        sent = chunks[(me + shift) % count]
        pairs = [(i, (i + shift) % count) for i in range(count)]
        total = total + lax.ppermute(sent, axis, pairs)
    return total


def local(tokens, cotangent, up_values, up_index, up_count, down_values, down_index, down_count):
    block_size = up_values.shape[-1]
    tile_rows = tokens.shape[1]
    block_rows = tile_rows // block_size
    block_cols = FF // (block_size * lax.axis_size(("col", "seq")))
    up_vals = up_values[0, 0]
    up_chosen = up_index[0, 0]
    up_rowblk = up_chosen // block_cols
    up_colblk = up_chosen % block_cols
    down_vals = down_values[0, 0]
    down_chosen = down_index[0, 0]
    down_rowblk = down_chosen // block_cols
    down_colblk = down_chosen % block_cols
    up_n = up_count[0, 0]
    down_n = down_count[0, 0]

    stacked = jnp.stack([tokens, cotangent])
    local_rows = stacked.shape[1]
    blocked = stacked.reshape(2, local_rows, block_rows, block_size).transpose(0, 2, 1, 3)
    shard_rows = lax.all_gather(blocked, ("col", "seq"), axis=2, tiled=True)
    pre_part, grad_part = block_pass(
        shard_rows[0], up_vals, up_rowblk, up_colblk, up_n,
        shard_rows[1], down_vals, down_rowblk, down_colblk, down_n,
        block_cols, (False, True),
    )
    partial_value = jnp.stack([pre_part, grad_part])
    count_rows = partial_value.shape[2]
    partial_value = partial_value.transpose(2, 0, 1, 3).reshape(count_rows, 2, -1)
    shares = exchange_sum(partial_value, "row").transpose(1, 0, 2)
    activated = lax.all_gather(activate(shares), "row", axis=1, tiled=True)
    activated = activated.reshape(2, count_rows, block_cols, block_size).transpose(0, 2, 1, 3)
    out_part, back_part = block_pass(
        activated[0], down_vals, down_colblk, down_rowblk, down_n,
        activated[1], up_vals, up_colblk, up_rowblk, up_n,
        block_rows, (False, True),
    )
    final = jnp.stack([out_part, back_part]).transpose(2, 0, 1, 3).reshape(count_rows, 2, tile_rows)
    result = exchange_sum(final, ("col", "seq")).astype(jnp.bfloat16)
    return (result[:, 0], result[:, 1])


def solution(mesh):
    return jax.shard_map(
        local,
        mesh=mesh,
        in_specs=(
            P(("col", "seq"), "row"),
            P(("col", "seq"), "row"),
            P("row", ("col", "seq"), None, None, None),
            P("row", ("col", "seq"), None),
            P("row", ("col", "seq")),
            P("row", ("col", "seq"), None, None, None),
            P("row", ("col", "seq"), None),
            P("row", ("col", "seq")),
        ),
        out_specs=(P(("col", "seq"), "row"), P(("col", "seq"), "row")),
        check_vma=False,
    )
```

```python
import jax
import jax.numpy as jnp
from jax import lax
from jax.experimental import pallas as pl
from jax.experimental.pallas import tpu as pltpu
from jax.sharding import PartitionSpec as P

FF = 49152


def gelu_forward(inputs):
    return jax.nn.gelu(inputs, approximate=True)


def gelu_backward(pre_act, gradient):
    return jax.vjp(gelu_forward, pre_act)[1](gradient)[0]


def activate(paired):
    pre_act = paired[0]
    return jnp.stack(
        [
            gelu_forward(pre_act).astype(jnp.bfloat16),
            gelu_backward(pre_act, paired[1]).astype(jnp.bfloat16),
        ]
    )


def group_size(slots):
    best = 1
    for size in range(1, 97):
        if slots % size == 0:
            best = size
    return best


def block_kernel(group, block_cols, pick_row, flipped):
    def kernel(index, count, x, w, o):
        step = pl.program_id(0)
        first = step * group
        live = count[0]

        @pl.when(step == 0)
        def _():
            o[...] = jnp.zeros_like(o)

        @pl.when(first < live)
        def _():
            for j in range(group):
                slot = first + j
                code = index[slot]
                row = lax.div(code, block_cols)
                col = code - row * block_cols
                src = x[row if pick_row else col]
                blk = w[j]
                if flipped:
                    prod = lax.dot_general(
                        src, blk, (((1,), (1,)), ((), ())),
                        preferred_element_type=jnp.float32,
                    )
                else:
                    prod = jnp.dot(src, blk, preferred_element_type=jnp.float32)
                scale = jnp.where(slot < live, 1.0, 0.0).astype(jnp.float32)
                dst = col if pick_row else row
                o[dst] = o[dst] + prod * scale

    return kernel


def block_pass(x, w, index, count, block_cols, pick_row, flipped, out_blocks):
    slots, blk, _ = w.shape
    rows = x.shape[1]
    group = group_size(slots)

    def w_map(i, index, count):
        last = jnp.maximum(count[0] - 1, 0) // group
        return (jnp.minimum(i, last), 0, 0)

    spec = pltpu.PrefetchScalarGridSpec(
        num_scalar_prefetch=2,
        grid=(slots // group,),
        in_specs=[
            pl.BlockSpec(x.shape, lambda i, index, count: (0, 0, 0)),
            pl.BlockSpec((group, blk, blk), w_map),
        ],
        out_specs=pl.BlockSpec((out_blocks, rows, blk), lambda i, index, count: (0, 0, 0)),
    )
    return pl.pallas_call(
        block_kernel(group, block_cols, pick_row, flipped),
        grid_spec=spec,
        out_shape=jax.ShapeDtypeStruct((out_blocks, rows, blk), jnp.float32),
        compiler_params=pltpu.CompilerParams(dimension_semantics=("arbitrary",)),
    )(index, count, x, w)


def exchange_sum(x, axis):
    count = lax.axis_size(axis)
    me = lax.axis_index(axis)
    chunks = x.reshape((count, x.shape[0] // count) + x.shape[1:])
    total = chunks[me]
    for shift in range(1, count):
        sent = chunks[(me + shift) % count]
        pairs = [(i, (i + shift) % count) for i in range(count)]
        total = total + lax.ppermute(sent, axis, pairs)
    return total


def local(tokens, cotangent, up_values, up_index, up_count, down_values, down_index, down_count):
    block_size = up_values.shape[-1]
    tile_rows = tokens.shape[1]
    block_rows = tile_rows // block_size
    block_cols = FF // (block_size * lax.axis_size(("col", "seq")))
    up_vals = up_values[0, 0]
    up_codes = up_index[0, 0]
    up_n = up_count.reshape(1)
    down_vals = down_values[0, 0]
    down_codes = down_index[0, 0]
    down_n = down_count.reshape(1)
    local_rows = tokens.shape[0]

    def gather_rows(part):
        blocked = part.reshape(local_rows, block_rows, block_size).transpose(1, 0, 2)
        return lax.all_gather(blocked, ("col", "seq"), axis=1, tiled=True)

    def row_sum(part):
        count_rows = part.shape[1]
        flat = part.transpose(1, 0, 2).reshape(count_rows, -1)
        return exchange_sum(flat, "row")

    def col_sum(part):
        count_rows = part.shape[1]
        flat = part.transpose(1, 0, 2).reshape(count_rows, -1)
        return exchange_sum(flat, ("col", "seq"))

    tok_rows = gather_rows(tokens)
    pre_part = block_pass(tok_rows, up_vals, up_codes, up_n, block_cols, True, False, block_cols)
    pre_share = row_sum(pre_part)
    cot_rows = gather_rows(cotangent)
    grad_part = block_pass(cot_rows, down_vals, down_codes, down_n, block_cols, True, True, block_cols)
    grad_share = row_sum(grad_part)
    activated = activate(jnp.stack([pre_share, grad_share]))
    count_rows = pre_part.shape[1]

    def gather_hidden(part):
        full = lax.all_gather(part, "row", axis=0, tiled=True)
        return full.reshape(count_rows, block_cols, block_size).transpose(1, 0, 2)

    act_rows = gather_hidden(activated[0])
    out_part = block_pass(act_rows, down_vals, down_codes, down_n, block_cols, False, False, block_rows)
    out_share = col_sum(out_part)
    gp_rows = gather_hidden(activated[1])
    back_part = block_pass(gp_rows, up_vals, up_codes, up_n, block_cols, False, True, block_rows)
    back_share = col_sum(back_part)
    return (out_share.astype(jnp.bfloat16), back_share.astype(jnp.bfloat16))


def solution(mesh):
    return jax.shard_map(
        local,
        mesh=mesh,
        in_specs=(
            P(("col", "seq"), "row"),
            P(("col", "seq"), "row"),
            P("row", ("col", "seq"), None, None, None),
            P("row", ("col", "seq"), None),
            P("row", ("col", "seq")),
            P("row", ("col", "seq"), None, None, None),
            P("row", ("col", "seq"), None),
            P("row", ("col", "seq")),
        ),
        out_specs=(P(("col", "seq"), "row"), P(("col", "seq"), "row")),
        check_vma=False,
    )
```

```python
import jax
import jax.numpy as jnp
from jax import lax
from jax.experimental import pallas as pl
from jax.experimental.pallas import tpu as pltpu
from jax.sharding import PartitionSpec as P

FF = 49152


def gelu_forward(inputs):
    return jax.nn.gelu(inputs, approximate=True)


def gelu_backward(pre_act, gradient):
    return jax.vjp(gelu_forward, pre_act)[1](gradient)[0]


def activate(paired):
    pre_act = paired[0]
    return jnp.stack(
        [
            gelu_forward(pre_act).astype(jnp.bfloat16),
            gelu_backward(pre_act, paired[1]).astype(jnp.bfloat16),
        ]
    )


def group_size(slots):
    best = 1
    for size in range(1, 97):
        if slots % size == 0:
            best = size
    return best


def block_kernel(group, block_cols, pick_row, flips):
    def kernel(codes0, codes1, counts, x0, x1, w0, w1, o0, o1):
        step = pl.program_id(0)
        first = step * group

        @pl.when(step == 0)
        def _():
            o0[...] = jnp.zeros_like(o0)
            o1[...] = jnp.zeros_like(o1)

        streams = ((codes0, x0, w0, o0, flips[0], 0), (codes1, x1, w1, o1, flips[1], 1))
        for codes, x, w, o, flipped, which in streams:
            live = counts[which]

            @pl.when(first < live)
            def _(codes=codes, x=x, w=w, o=o, flipped=flipped, live=live):
                for j in range(group):
                    slot = first + j
                    code = codes[slot]
                    row = lax.div(code, block_cols)
                    col = code - row * block_cols
                    src = x[row if pick_row else col]
                    blk = w[j]
                    if flipped:
                        prod = lax.dot_general(
                            src, blk, (((1,), (1,)), ((), ())),
                            preferred_element_type=jnp.float32,
                        )
                    else:
                        prod = jnp.dot(src, blk, preferred_element_type=jnp.float32)
                    scale = jnp.where(slot < live, 1.0, 0.0).astype(jnp.float32)
                    dst = col if pick_row else row
                    o[dst] = o[dst] + prod * scale

    return kernel


def block_pass(x0, w0, codes0, x1, w1, codes1, counts, block_cols, pick_row, out_blocks, flips):
    slots, blk, _ = w0.shape
    rows = x0.shape[1]
    group = group_size(slots)

    def w_map(which):
        def index_map(i, c0, c1, c):
            last = jnp.maximum(c[which] - 1, 0) // group
            return (jnp.minimum(i, last), 0, 0)

        return index_map

    def whole(shape):
        return pl.BlockSpec(shape, lambda i, c0, c1, c: (0, 0, 0))

    spec = pltpu.PrefetchScalarGridSpec(
        num_scalar_prefetch=3,
        grid=(slots // group,),
        in_specs=[
            whole(x0.shape),
            whole(x1.shape),
            pl.BlockSpec((group, blk, blk), w_map(0)),
            pl.BlockSpec((group, blk, blk), w_map(1)),
        ],
        out_specs=[
            whole((out_blocks, rows, blk)),
            whole((out_blocks, rows, blk)),
        ],
    )
    out_shape = [jax.ShapeDtypeStruct((out_blocks, rows, blk), jnp.float32)] * 2
    return pl.pallas_call(
        block_kernel(group, block_cols, pick_row, flips),
        grid_spec=spec,
        out_shape=out_shape,
        compiler_params=pltpu.CompilerParams(dimension_semantics=("arbitrary",)),
    )(codes0, codes1, counts, x0, x1, w0, w1)


def exchange_sum(x, axis):
    count = lax.axis_size(axis)
    me = lax.axis_index(axis)
    chunks = x.reshape((count, x.shape[0] // count) + x.shape[1:])
    total = chunks[me]
    for shift in range(1, count):
        sent = chunks[(me + shift) % count]
        pairs = [(i, (i + shift) % count) for i in range(count)]
        total = total + lax.ppermute(sent, axis, pairs)
    return total


def local(tokens, cotangent, up_values, up_index, up_count, down_values, down_index, down_count):
    block_size = up_values.shape[-1]
    tile_rows = tokens.shape[1]
    block_rows = tile_rows // block_size
    block_cols = FF // (block_size * lax.axis_size(("col", "seq")))
    up_vals = up_values[0, 0]
    up_codes = up_index[0, 0]
    down_vals = down_values[0, 0]
    down_codes = down_index[0, 0]
    first_counts = jnp.concatenate([up_count.reshape(1), down_count.reshape(1)])
    second_counts = jnp.concatenate([down_count.reshape(1), up_count.reshape(1)])

    stacked = jnp.stack([tokens, cotangent])
    local_rows = stacked.shape[1]
    blocked = stacked.reshape(2, local_rows, block_rows, block_size).transpose(0, 2, 1, 3)
    shard_rows = lax.all_gather(blocked, ("col", "seq"), axis=2, tiled=True)
    pre_part, grad_part = block_pass(
        shard_rows[0], up_vals, up_codes, shard_rows[1], down_vals, down_codes,
        first_counts, block_cols, True, block_cols, (False, True),
    )
    partial_value = jnp.stack([pre_part, grad_part])
    count_rows = partial_value.shape[2]
    partial_value = partial_value.transpose(2, 0, 1, 3).reshape(count_rows, 2, -1)
    shares = exchange_sum(partial_value, "row").transpose(1, 0, 2)
    activated = lax.all_gather(activate(shares), "row", axis=1, tiled=True)
    activated = activated.reshape(2, count_rows, block_cols, block_size).transpose(0, 2, 1, 3)
    out_part, back_part = block_pass(
        activated[0], down_vals, down_codes, activated[1], up_vals, up_codes,
        second_counts, block_cols, False, block_rows, (False, True),
    )
    final = jnp.stack([out_part, back_part]).transpose(2, 0, 1, 3).reshape(count_rows, 2, tile_rows)
    result = exchange_sum(final, ("col", "seq")).astype(jnp.bfloat16)
    return (result[:, 0], result[:, 1])


def solution(mesh):
    return jax.shard_map(
        local,
        mesh=mesh,
        in_specs=(
            P(("col", "seq"), "row"),
            P(("col", "seq"), "row"),
            P("row", ("col", "seq"), None, None, None),
            P("row", ("col", "seq"), None),
            P("row", ("col", "seq")),
            P("row", ("col", "seq"), None, None, None),
            P("row", ("col", "seq"), None),
            P("row", ("col", "seq")),
        ),
        out_specs=(P(("col", "seq"), "row"), P(("col", "seq"), "row")),
        check_vma=False,
    )
```

```python
import jax
import jax.numpy as jnp
from jax import lax
from jax.experimental import pallas as pl
from jax.experimental.pallas import tpu as pltpu
from jax.sharding import PartitionSpec as P

FF = 49152


def gelu_forward(inputs):
    return jax.nn.gelu(inputs, approximate=True)


def gelu_backward(pre_act, gradient):
    return jax.vjp(gelu_forward, pre_act)[1](gradient)[0]


def activate(paired):
    pre_act = paired[0]
    return jnp.stack(
        [
            gelu_forward(pre_act).astype(jnp.bfloat16),
            gelu_backward(pre_act, paired[1]).astype(jnp.bfloat16),
        ]
    )


def group_size(slots):
    best = 1
    for size in range(1, 97):
        if slots % size == 0:
            best = size
    return best


def block_kernel(group, block_cols, pick_row, flips):
    def kernel(codes0, codes1, counts, x0, x1, w0, w1, o0, o1):
        step = pl.program_id(0)
        first = step * group

        @pl.when(step == 0)
        def _():
            o0[...] = jnp.zeros_like(o0)
            o1[...] = jnp.zeros_like(o1)

        streams = ((codes0, x0, w0, o0, flips[0], 0), (codes1, x1, w1, o1, flips[1], 1))
        for codes, x, w, o, flipped, which in streams:
            live = counts[which]

            @pl.when(first < live)
            def _(codes=codes, x=x, w=w, o=o, flipped=flipped, live=live):
                for j in range(group):
                    slot = first + j
                    code = codes[slot]
                    row = lax.div(code, block_cols)
                    col = code - row * block_cols
                    src = x[row if pick_row else col]
                    blk = w[j]
                    if flipped:
                        prod = lax.dot_general(
                            src, blk, (((1,), (1,)), ((), ())),
                            preferred_element_type=jnp.float32,
                        )
                    else:
                        prod = jnp.dot(src, blk, preferred_element_type=jnp.float32)
                    scale = jnp.where(slot < live, 1.0, 0.0).astype(jnp.float32)
                    dst = col if pick_row else row
                    o[dst] = o[dst] + prod * scale

    return kernel


def block_pass(x0, w0, codes0, x1, w1, codes1, counts, block_cols, pick_row, out_blocks, flips):
    slots, blk, _ = w0.shape
    rows = x0.shape[1]
    group = group_size(slots)

    def w_map(which):
        def index_map(i, c0, c1, c):
            last = jnp.maximum(c[which] - 1, 0) // group
            return (jnp.minimum(i, last), 0, 0)

        return index_map

    def whole(shape):
        return pl.BlockSpec(shape, lambda i, c0, c1, c: (0, 0, 0))

    spec = pltpu.PrefetchScalarGridSpec(
        num_scalar_prefetch=3,
        grid=(slots // group,),
        in_specs=[
            whole(x0.shape),
            whole(x1.shape),
            pl.BlockSpec((group, blk, blk), w_map(0)),
            pl.BlockSpec((group, blk, blk), w_map(1)),
        ],
        out_specs=[
            whole((out_blocks, rows, blk)),
            whole((out_blocks, rows, blk)),
        ],
    )
    out_shape = [jax.ShapeDtypeStruct((out_blocks, rows, blk), jnp.float32)] * 2
    return pl.pallas_call(
        block_kernel(group, block_cols, pick_row, flips),
        grid_spec=spec,
        out_shape=out_shape,
        compiler_params=pltpu.CompilerParams(dimension_semantics=("arbitrary",)),
    )(codes0, codes1, counts, x0, x1, w0, w1)


def exchange_sum(x, axis):
    count = lax.axis_size(axis)
    me = lax.axis_index(axis)
    chunks = x.reshape((count, x.shape[0] // count) + x.shape[1:])
    total = chunks[me]
    for shift in range(1, count):
        sent = chunks[(me + shift) % count]
        pairs = [(i, (i + shift) % count) for i in range(count)]
        total = total + lax.ppermute(sent, axis, pairs)
    return total


def local(tokens, cotangent, up_values, up_index, up_count, down_values, down_index, down_count):
    block_size = up_values.shape[-1]
    tile_rows = tokens.shape[1]
    block_rows = tile_rows // block_size
    block_cols = FF // (block_size * lax.axis_size(("col", "seq")))
    up_vals = up_values[0, 0]
    up_codes = up_index[0, 0]
    down_vals = down_values[0, 0]
    down_codes = down_index[0, 0]
    first_counts = jnp.concatenate([up_count.reshape(1), down_count.reshape(1)])
    second_counts = jnp.concatenate([down_count.reshape(1), up_count.reshape(1)])

    stacked = jnp.stack([tokens, cotangent])
    local_rows = stacked.shape[1]
    blocked = stacked.reshape(2, local_rows, block_rows, block_size).transpose(0, 2, 1, 3)
    shard_rows = lax.all_gather(blocked, ("col", "seq"), axis=2, tiled=True)
    pre_part, grad_part = block_pass(
        shard_rows[0], up_vals, up_codes, shard_rows[1], down_vals, down_codes,
        first_counts, block_cols, True, block_cols, (False, True),
    )
    partial_value = jnp.stack([pre_part, grad_part])
    count_rows = partial_value.shape[2]
    partial_value = partial_value.transpose(2, 0, 1, 3).reshape(count_rows, 2, -1)
    shares = exchange_sum(partial_value, "row").transpose(1, 0, 2)
    activated = lax.all_gather(activate(shares), "row", axis=1, tiled=True)
    activated = activated.reshape(2, count_rows, block_cols, block_size).transpose(0, 2, 1, 3)
    out_part, back_part = block_pass(
        activated[0], down_vals, down_codes, activated[1], up_vals, up_codes,
        second_counts, block_cols, False, block_rows, (False, True),
    )
    col_count = lax.axis_size("col")
    seq_count = lax.axis_size("seq")
    final = jnp.stack([out_part, back_part]).transpose(2, 0, 1, 3)
    final = final.reshape(col_count, seq_count, local_rows, 2, tile_rows).transpose(1, 0, 2, 3, 4)
    chip_sum = exchange_sum(final.reshape(count_rows, 2, tile_rows), "seq")
    result = exchange_sum(chip_sum, "col").astype(jnp.bfloat16)
    return (result[:, 0], result[:, 1])


def solution(mesh):
    return jax.shard_map(
        local,
        mesh=mesh,
        in_specs=(
            P(("col", "seq"), "row"),
            P(("col", "seq"), "row"),
            P("row", ("col", "seq"), None, None, None),
            P("row", ("col", "seq"), None),
            P("row", ("col", "seq")),
            P("row", ("col", "seq"), None, None, None),
            P("row", ("col", "seq"), None),
            P("row", ("col", "seq")),
        ),
        out_specs=(P(("col", "seq"), "row"), P(("col", "seq"), "row")),
        check_vma=False,
    )
```

```python
import jax
import jax.numpy as jnp
from jax import lax
from jax.experimental import pallas as pl
from jax.experimental.pallas import tpu as pltpu
from jax.sharding import PartitionSpec as P

FF = 49152


def gelu_forward(inputs):
    return jax.nn.gelu(inputs, approximate=True)


def gelu_backward(pre_act, gradient):
    return jax.vjp(gelu_forward, pre_act)[1](gradient)[0]


def activate(paired):
    pre_act = paired[0]
    return jnp.stack(
        [
            gelu_forward(pre_act).astype(jnp.bfloat16),
            gelu_backward(pre_act, paired[1]).astype(jnp.bfloat16),
        ]
    )


def group_size(slots):
    best = 1
    for size in range(1, 97):
        if slots % size == 0:
            best = size
    return best


def block_kernel(group, block_cols, pick_row, flips):
    def kernel(codes0, codes1, count0, count1, x, w0, w1, o0, o1):
        step = pl.program_id(0)
        first = step * group

        @pl.when(step == 0)
        def _():
            o0[...] = jnp.zeros_like(o0)
            o1[...] = jnp.zeros_like(o1)

        streams = ((codes0, count0, w0, o0, flips[0], 0), (codes1, count1, w1, o1, flips[1], 1))
        for codes, count, w, o, flipped, which in streams:
            live = count[0, 0]

            @pl.when(first < live)
            def _(codes=codes, w=w, o=o, flipped=flipped, live=live, which=which):
                for j in range(group):
                    slot = first + j
                    code = codes[0, 0, slot]
                    row = lax.div(code, block_cols)
                    col = code - row * block_cols
                    src = x[which, row if pick_row else col]
                    blk = w[j]
                    if flipped:
                        prod = lax.dot_general(
                            src, blk, (((1,), (1,)), ((), ())),
                            preferred_element_type=jnp.float32,
                        )
                    else:
                        prod = jnp.dot(src, blk, preferred_element_type=jnp.float32)
                    scale = jnp.where(slot < live, 1.0, 0.0).astype(jnp.float32)
                    dst = col if pick_row else row
                    o[dst] = o[dst] + prod * scale

    return kernel


def block_pass(x, w0, codes0, count0, w1, codes1, count1, block_cols, pick_row, out_blocks, flips):
    slots, blk, _ = w0.shape
    rows = x.shape[2]
    group = group_size(slots)

    def w_map(which):
        def index_map(i, c0, c1, n0, n1):
            live = (n0, n1)[which][0, 0]
            last = jnp.maximum(live - 1, 0) // group
            return (jnp.minimum(i, last), 0, 0)

        return index_map

    def whole(shape):
        return pl.BlockSpec(shape, lambda i, *refs: (0,) * len(shape))

    spec = pltpu.PrefetchScalarGridSpec(
        num_scalar_prefetch=4,
        grid=(slots // group,),
        in_specs=[
            whole(x.shape),
            pl.BlockSpec((group, blk, blk), w_map(0)),
            pl.BlockSpec((group, blk, blk), w_map(1)),
        ],
        out_specs=[
            whole((out_blocks, rows, blk)),
            whole((out_blocks, rows, blk)),
        ],
    )
    out_shape = [jax.ShapeDtypeStruct((out_blocks, rows, blk), jnp.float32)] * 2
    return pl.pallas_call(
        block_kernel(group, block_cols, pick_row, flips),
        grid_spec=spec,
        out_shape=out_shape,
        compiler_params=pltpu.CompilerParams(dimension_semantics=("arbitrary",)),
    )(codes0, codes1, count0, count1, x, w0, w1)


def exchange_sum(x, axis):
    count = lax.axis_size(axis)
    me = lax.axis_index(axis)
    chunks = x.reshape((count, x.shape[0] // count) + x.shape[1:])
    total = chunks[me]
    for shift in range(1, count):
        sent = chunks[(me + shift) % count]
        pairs = [(i, (i + shift) % count) for i in range(count)]
        total = total + lax.ppermute(sent, axis, pairs)
    return total


def local(tokens, cotangent, up_values, up_index, up_count, down_values, down_index, down_count):
    block_size = up_values.shape[-1]
    tile_rows = tokens.shape[1]
    block_rows = tile_rows // block_size
    block_cols = FF // (block_size * lax.axis_size(("col", "seq")))
    up_vals = up_values[0, 0]
    down_vals = down_values[0, 0]

    stacked = jnp.stack([tokens, cotangent])
    local_rows = stacked.shape[1]
    blocked = stacked.reshape(2, local_rows, block_rows, block_size).transpose(0, 2, 1, 3)
    shard_rows = lax.all_gather(blocked, ("col", "seq"), axis=2, tiled=True)
    pre_part, grad_part = block_pass(
        shard_rows, up_vals, up_index, up_count, down_vals, down_index, down_count,
        block_cols, True, block_cols, (False, True),
    )
    partial_value = jnp.stack([pre_part, grad_part])
    count_rows = partial_value.shape[2]
    partial_value = partial_value.transpose(2, 0, 1, 3).reshape(count_rows, 2, -1)
    shares = exchange_sum(partial_value, "row").transpose(1, 0, 2)
    activated = lax.all_gather(activate(shares), "row", axis=1, tiled=True)
    activated = activated.reshape(2, count_rows, block_cols, block_size).transpose(0, 2, 1, 3)
    out_part, back_part = block_pass(
        activated, down_vals, down_index, down_count, up_vals, up_index, up_count,
        block_cols, False, block_rows, (False, True),
    )
    col_count = lax.axis_size("col")
    seq_count = lax.axis_size("seq")
    final = jnp.stack([out_part, back_part]).transpose(2, 0, 1, 3)
    final = final.reshape(col_count, seq_count, local_rows, 2, tile_rows).transpose(1, 0, 2, 3, 4)
    chip_sum = exchange_sum(final.reshape(count_rows, 2, tile_rows), "seq")
    result = exchange_sum(chip_sum, "col").astype(jnp.bfloat16)
    return (result[:, 0], result[:, 1])


def solution(mesh):
    return jax.shard_map(
        local,
        mesh=mesh,
        in_specs=(
            P(("col", "seq"), "row"),
            P(("col", "seq"), "row"),
            P("row", ("col", "seq"), None, None, None),
            P("row", ("col", "seq"), None),
            P("row", ("col", "seq")),
            P("row", ("col", "seq"), None, None, None),
            P("row", ("col", "seq"), None),
            P("row", ("col", "seq")),
        ),
        out_specs=(P(("col", "seq"), "row"), P(("col", "seq"), "row")),
        check_vma=False,
    )
```

```python
import jax
import jax.numpy as jnp
from jax import lax
from jax.experimental import pallas as pl
from jax.experimental.pallas import tpu as pltpu
from jax.sharding import PartitionSpec as P

FF = 49152


def gelu_forward(inputs):
    return jax.nn.gelu(inputs, approximate=True)


def gelu_backward(pre_act, gradient):
    return jax.vjp(gelu_forward, pre_act)[1](gradient)[0]


def activate(paired):
    pre_act = paired[0]
    return jnp.stack(
        [
            gelu_forward(pre_act).astype(jnp.bfloat16),
            gelu_backward(pre_act, paired[1]).astype(jnp.bfloat16),
        ]
    )


def group_size(slots):
    best = 1
    for size in range(1, 97):
        if slots % size == 0:
            best = size
    return best


def block_kernel(group, block_cols, pick_row, flips):
    def kernel(codes0, codes1, count0, count1, x, w0, w1, o0, o1):
        step = pl.program_id(0)
        first = step * group

        @pl.when(step == 0)
        def _():
            o0[...] = jnp.zeros_like(o0)
            o1[...] = jnp.zeros_like(o1)

        streams = ((codes0, count0, w0, o0, flips[0], 0), (codes1, count1, w1, o1, flips[1], 1))
        for codes, count, w, o, flipped, which in streams:
            live = count[0, 0]

            @pl.when(first < live)
            def _(codes=codes, w=w, o=o, flipped=flipped, live=live, which=which):
                for j in range(group):
                    slot = first + j
                    code = codes[0, 0, slot]
                    row = lax.div(code, block_cols)
                    col = code - row * block_cols
                    src = x[which, row if pick_row else col]
                    blk = w[j]
                    if flipped:
                        prod = lax.dot_general(
                            src, blk, (((1,), (1,)), ((), ())),
                            preferred_element_type=jnp.float32,
                        )
                    else:
                        prod = jnp.dot(src, blk, preferred_element_type=jnp.float32)
                    scale = jnp.where(slot < live, 1.0, 0.0).astype(jnp.float32)
                    dst = col if pick_row else row
                    o[dst] = o[dst] + prod * scale

    return kernel


def block_pass(x, w0, codes0, count0, w1, codes1, count1, block_cols, pick_row, out_blocks, flips):
    slots, blk, _ = w0.shape
    rows = x.shape[2]
    group = group_size(slots)

    def w_map(which):
        def index_map(i, c0, c1, n0, n1):
            live = (n0, n1)[which][0, 0]
            last = jnp.maximum(live - 1, 0) // group
            return (jnp.minimum(i, last), 0, 0)

        return index_map

    def whole(shape):
        return pl.BlockSpec(shape, lambda i, *refs: (0,) * len(shape))

    spec = pltpu.PrefetchScalarGridSpec(
        num_scalar_prefetch=4,
        grid=(slots // group,),
        in_specs=[
            whole(x.shape),
            pl.BlockSpec((group, blk, blk), w_map(0)),
            pl.BlockSpec((group, blk, blk), w_map(1)),
        ],
        out_specs=[
            whole((out_blocks, rows, blk)),
            whole((out_blocks, rows, blk)),
        ],
    )
    out_shape = [jax.ShapeDtypeStruct((out_blocks, rows, blk), jnp.float32)] * 2
    return pl.pallas_call(
        block_kernel(group, block_cols, pick_row, flips),
        grid_spec=spec,
        out_shape=out_shape,
        compiler_params=pltpu.CompilerParams(dimension_semantics=("arbitrary",)),
    )(codes0, codes1, count0, count1, x, w0, w1)


def exchange_sum(x, axis, wire=jnp.float32):
    count = lax.axis_size(axis)
    me = lax.axis_index(axis)
    chunks = x.reshape((count, x.shape[0] // count) + x.shape[1:])
    total = chunks[me]
    for shift in range(1, count):
        sent = chunks[(me + shift) % count].astype(wire)
        pairs = [(i, (i + shift) % count) for i in range(count)]
        total = total + lax.ppermute(sent, axis, pairs).astype(jnp.float32)
    return total


def local(tokens, cotangent, up_values, up_index, up_count, down_values, down_index, down_count):
    block_size = up_values.shape[-1]
    tile_rows = tokens.shape[1]
    block_rows = tile_rows // block_size
    block_cols = FF // (block_size * lax.axis_size(("col", "seq")))
    up_vals = up_values[0, 0]
    down_vals = down_values[0, 0]

    stacked = jnp.stack([tokens, cotangent])
    local_rows = stacked.shape[1]
    blocked = stacked.reshape(2, local_rows, block_rows, block_size).transpose(0, 2, 1, 3)
    shard_rows = lax.all_gather(blocked, ("col", "seq"), axis=2, tiled=True)
    pre_part, grad_part = block_pass(
        shard_rows, up_vals, up_index, up_count, down_vals, down_index, down_count,
        block_cols, True, block_cols, (False, True),
    )
    count_rows = pre_part.shape[1]
    pre_flat = pre_part.transpose(1, 0, 2).reshape(count_rows, -1)
    grad_flat = grad_part.transpose(1, 0, 2).reshape(count_rows, -1)
    shares = jnp.stack(
        [exchange_sum(pre_flat, "row"), exchange_sum(grad_flat, "row", jnp.bfloat16)]
    )
    activated = lax.all_gather(activate(shares), "row", axis=1, tiled=True)
    activated = activated.reshape(2, count_rows, block_cols, block_size).transpose(0, 2, 1, 3)
    out_part, back_part = block_pass(
        activated, down_vals, down_index, down_count, up_vals, up_index, up_count,
        block_cols, False, block_rows, (False, True),
    )
    col_count = lax.axis_size("col")
    seq_count = lax.axis_size("seq")
    final = jnp.stack([out_part, back_part]).transpose(2, 0, 1, 3)
    final = final.reshape(col_count, seq_count, local_rows, 2, tile_rows).transpose(1, 0, 2, 3, 4)
    chip_sum = exchange_sum(final.reshape(count_rows, 2, tile_rows), "seq")
    result = exchange_sum(chip_sum, "col").astype(jnp.bfloat16)
    return (result[:, 0], result[:, 1])


def solution(mesh):
    return jax.shard_map(
        local,
        mesh=mesh,
        in_specs=(
            P(("col", "seq"), "row"),
            P(("col", "seq"), "row"),
            P("row", ("col", "seq"), None, None, None),
            P("row", ("col", "seq"), None),
            P("row", ("col", "seq")),
            P("row", ("col", "seq"), None, None, None),
            P("row", ("col", "seq"), None),
            P("row", ("col", "seq")),
        ),
        out_specs=(P(("col", "seq"), "row"), P(("col", "seq"), "row")),
        check_vma=False,
    )
```

```python
import jax
import jax.numpy as jnp
from jax import lax
from jax.experimental import pallas as pl
from jax.experimental.pallas import tpu as pltpu
from jax.sharding import PartitionSpec as P

FF = 49152


def gelu_forward(inputs):
    return jax.nn.gelu(inputs, approximate=True)


def gelu_backward(pre_act, gradient):
    return jax.vjp(gelu_forward, pre_act)[1](gradient)[0]


def activate(paired):
    pre_act = paired[0]
    return jnp.stack(
        [
            gelu_forward(pre_act).astype(jnp.bfloat16),
            gelu_backward(pre_act, paired[1]).astype(jnp.bfloat16),
        ]
    )


def group_size(slots):
    best = 1
    for size in range(1, 97):
        if slots % size == 0:
            best = size
    return best


def block_kernel(group, block_cols, pick_row, flips, blk_size):
    def kernel(codes0, codes1, count0, count1, x, w0, w1, o0, o1):
        step = pl.program_id(0)
        first = step * group

        @pl.when(step == 0)
        def _():
            o0[...] = jnp.zeros_like(o0)
            o1[...] = jnp.zeros_like(o1)

        streams = ((codes0, count0, w0, o0, flips[0], 0), (codes1, count1, w1, o1, flips[1], 1))
        for codes, count, w, o, flipped, which in streams:
            live = count[0, 0]

            @pl.when(first < live)
            def _(codes=codes, w=w, o=o, flipped=flipped, live=live, which=which):
                for j in range(group):
                    slot = first + j
                    code = codes[0, 0, slot]
                    row = lax.div(code, block_cols)
                    col = code - row * block_cols
                    pick = row if pick_row else col
                    src = x[which, :, pl.ds(pl.multiple_of(pick * blk_size, blk_size), blk_size)]
                    blk = w[j]
                    if flipped:
                        prod = lax.dot_general(
                            src, blk, (((1,), (1,)), ((), ())),
                            preferred_element_type=jnp.float32,
                        )
                    else:
                        prod = jnp.dot(src, blk, preferred_element_type=jnp.float32)
                    scale = jnp.where(slot < live, 1.0, 0.0).astype(jnp.float32)
                    dst = col if pick_row else row
                    lanes = pl.ds(pl.multiple_of(dst * blk_size, blk_size), blk_size)
                    o[:, lanes] = o[:, lanes] + prod * scale

    return kernel


def block_pass(x, w0, codes0, count0, w1, codes1, count1, block_cols, pick_row, out_blocks, flips):
    slots, blk, _ = w0.shape
    rows = x.shape[1]
    group = group_size(slots)

    def w_map(which):
        def index_map(i, c0, c1, n0, n1):
            live = (n0, n1)[which][0, 0]
            last = jnp.maximum(live - 1, 0) // group
            return (jnp.minimum(i, last), 0, 0)

        return index_map

    def whole(shape):
        return pl.BlockSpec(shape, lambda i, *refs: (0,) * len(shape))

    spec = pltpu.PrefetchScalarGridSpec(
        num_scalar_prefetch=4,
        grid=(slots // group,),
        in_specs=[
            whole(x.shape),
            pl.BlockSpec((group, blk, blk), w_map(0)),
            pl.BlockSpec((group, blk, blk), w_map(1)),
        ],
        out_specs=[
            whole((rows, out_blocks * blk)),
            whole((rows, out_blocks * blk)),
        ],
    )
    out_shape = [jax.ShapeDtypeStruct((rows, out_blocks * blk), jnp.float32)] * 2
    return pl.pallas_call(
        block_kernel(group, block_cols, pick_row, flips, blk),
        grid_spec=spec,
        out_shape=out_shape,
        compiler_params=pltpu.CompilerParams(dimension_semantics=("arbitrary",)),
    )(codes0, codes1, count0, count1, x, w0, w1)


def exchange_sum(x, axis, wire=jnp.float32):
    count = lax.axis_size(axis)
    me = lax.axis_index(axis)
    chunks = x.reshape((count, x.shape[0] // count) + x.shape[1:])
    total = chunks[me]
    for shift in range(1, count):
        sent = chunks[(me + shift) % count].astype(wire)
        pairs = [(i, (i + shift) % count) for i in range(count)]
        total = total + lax.ppermute(sent, axis, pairs).astype(jnp.float32)
    return total


def local(tokens, cotangent, up_values, up_index, up_count, down_values, down_index, down_count):
    block_size = up_values.shape[-1]
    tile_rows = tokens.shape[1]
    block_rows = tile_rows // block_size
    block_cols = FF // (block_size * lax.axis_size(("col", "seq")))
    up_vals = up_values[0, 0]
    down_vals = down_values[0, 0]

    stacked = jnp.stack([tokens, cotangent])
    local_rows = stacked.shape[1]
    shard_rows = lax.all_gather(stacked, ("col", "seq"), axis=1, tiled=True)
    pre_part, grad_part = block_pass(
        shard_rows, up_vals, up_index, up_count, down_vals, down_index, down_count,
        block_cols, True, block_cols, (False, True),
    )
    count_rows = pre_part.shape[0]
    shares = jnp.stack(
        [exchange_sum(pre_part, "row"), exchange_sum(grad_part, "row", jnp.bfloat16)]
    )
    activated = lax.all_gather(activate(shares), "row", axis=1, tiled=True)
    out_part, back_part = block_pass(
        activated, down_vals, down_index, down_count, up_vals, up_index, up_count,
        block_cols, False, block_rows, (False, True),
    )
    col_count = lax.axis_size("col")
    seq_count = lax.axis_size("seq")
    final = jnp.stack([out_part, back_part], axis=1)
    final = final.reshape(col_count, seq_count, local_rows, 2, tile_rows).transpose(1, 0, 2, 3, 4)
    chip_sum = exchange_sum(final.reshape(count_rows, 2, tile_rows), "seq")
    result = exchange_sum(chip_sum, "col").astype(jnp.bfloat16)
    return (result[:, 0], result[:, 1])


def solution(mesh):
    return jax.shard_map(
        local,
        mesh=mesh,
        in_specs=(
            P(("col", "seq"), "row"),
            P(("col", "seq"), "row"),
            P("row", ("col", "seq"), None, None, None),
            P("row", ("col", "seq"), None),
            P("row", ("col", "seq")),
            P("row", ("col", "seq"), None, None, None),
            P("row", ("col", "seq"), None),
            P("row", ("col", "seq")),
        ),
        out_specs=(P(("col", "seq"), "row"), P(("col", "seq"), "row")),
        check_vma=False,
    )
```

```python
import jax
import jax.numpy as jnp
from jax import lax
from jax.experimental import pallas as pl
from jax.experimental.pallas import tpu as pltpu
from jax.sharding import PartitionSpec as P

FF = 49152


def gelu_forward(inputs):
    return jax.nn.gelu(inputs, approximate=True)


def gelu_backward(pre_act, gradient):
    return jax.vjp(gelu_forward, pre_act)[1](gradient)[0]


def activate(paired):
    pre_act = paired[0]
    return jnp.stack(
        [
            gelu_forward(pre_act).astype(jnp.bfloat16),
            gelu_backward(pre_act, paired[1]).astype(jnp.bfloat16),
        ]
    )


def group_size(slots):
    best = 1
    for size in range(1, 97):
        if slots % size == 0:
            best = size
    return best


def block_kernel(group, block_cols, pick_row, flips):
    def kernel(codes0, codes1, count0, count1, x, w0, w1, o0, o1):
        step = pl.program_id(0)
        first = step * group

        @pl.when(step == 0)
        def _():
            o0[...] = jnp.zeros_like(o0)
            o1[...] = jnp.zeros_like(o1)

        streams = ((codes0, count0, w0, o0, flips[0], 0), (codes1, count1, w1, o1, flips[1], 1))
        for codes, count, w, o, flipped, which in streams:
            live = count[0, 0]

            @pl.when(first < live)
            def _(codes=codes, w=w, o=o, flipped=flipped, live=live, which=which):
                for j in range(group):
                    slot = first + j
                    code = codes[0, 0, slot]
                    row = lax.div(code, block_cols)
                    col = code - row * block_cols
                    src = x[which, row if pick_row else col]
                    blk = w[j]
                    if flipped:
                        prod = lax.dot_general(
                            src, blk, (((1,), (1,)), ((), ())),
                            preferred_element_type=jnp.float32,
                        )
                    else:
                        prod = jnp.dot(src, blk, preferred_element_type=jnp.float32)
                    scale = jnp.where(slot < live, 1.0, 0.0).astype(jnp.float32)
                    dst = col if pick_row else row
                    o[dst] = o[dst] + prod * scale

    return kernel


def block_pass(x, w0, codes0, count0, w1, codes1, count1, block_cols, pick_row, out_blocks, flips):
    slots, blk, _ = w0.shape
    rows = x.shape[2]
    group = group_size(slots)

    def w_map(which):
        def index_map(i, c0, c1, n0, n1):
            live = (n0, n1)[which][0, 0]
            last = jnp.maximum(live - 1, 0) // group
            return (jnp.minimum(i, last), 0, 0)

        return index_map

    def whole(shape):
        return pl.BlockSpec(shape, lambda i, *refs: (0,) * len(shape))

    spec = pltpu.PrefetchScalarGridSpec(
        num_scalar_prefetch=4,
        grid=(slots // group,),
        in_specs=[
            whole(x.shape),
            pl.BlockSpec((group, blk, blk), w_map(0)),
            pl.BlockSpec((group, blk, blk), w_map(1)),
        ],
        out_specs=[
            whole((out_blocks, rows, blk)),
            whole((out_blocks, rows, blk)),
        ],
    )
    out_shape = [jax.ShapeDtypeStruct((out_blocks, rows, blk), jnp.float32)] * 2
    return pl.pallas_call(
        block_kernel(group, block_cols, pick_row, flips),
        grid_spec=spec,
        out_shape=out_shape,
        compiler_params=pltpu.CompilerParams(dimension_semantics=("arbitrary",)),
    )(codes0, codes1, count0, count1, x, w0, w1)


def exchange_sum(x, axis, wire=jnp.float32):
    count = lax.axis_size(axis)
    me = lax.axis_index(axis)
    chunks = x.reshape((count, x.shape[0] // count) + x.shape[1:])
    total = chunks[me]
    for shift in range(1, count):
        sent = chunks[(me + shift) % count].astype(wire)
        pairs = [(i, (i + shift) % count) for i in range(count)]
        total = total + lax.ppermute(sent, axis, pairs).astype(jnp.float32)
    return total


def exchange_blocks(x, axis, wire=jnp.float32):
    count = lax.axis_size(axis)
    me = lax.axis_index(axis)
    width = x.shape[1] // count

    def chunk(index):
        return lax.dynamic_slice_in_dim(x, index * width, width, axis=1)

    total = chunk(me)
    for shift in range(1, count):
        sent = chunk((me + shift) % count).astype(wire)
        pairs = [(i, (i + shift) % count) for i in range(count)]
        total = total + lax.ppermute(sent, axis, pairs).astype(jnp.float32)
    return total


def local(tokens, cotangent, up_values, up_index, up_count, down_values, down_index, down_count):
    block_size = up_values.shape[-1]
    tile_rows = tokens.shape[1]
    block_rows = tile_rows // block_size
    block_cols = FF // (block_size * lax.axis_size(("col", "seq")))
    up_vals = up_values[0, 0]
    down_vals = down_values[0, 0]

    stacked = jnp.stack([tokens, cotangent])
    local_rows = stacked.shape[1]
    blocked = stacked.reshape(2, local_rows, block_rows, block_size).transpose(0, 2, 1, 3)
    shard_rows = lax.all_gather(blocked, ("col", "seq"), axis=2, tiled=True)
    pre_part, grad_part = block_pass(
        shard_rows, up_vals, up_index, up_count, down_vals, down_index, down_count,
        block_cols, True, block_cols, (False, True),
    )
    count_rows = pre_part.shape[1]
    shares = jnp.stack(
        [exchange_blocks(pre_part, "row"), exchange_blocks(grad_part, "row", jnp.bfloat16)]
    )
    activated = lax.all_gather(activate(shares), "row", axis=2, tiled=True)
    out_part, back_part = block_pass(
        activated, down_vals, down_index, down_count, up_vals, up_index, up_count,
        block_cols, False, block_rows, (False, True),
    )
    col_count = lax.axis_size("col")
    seq_count = lax.axis_size("seq")
    final = jnp.stack([out_part, back_part]).transpose(2, 0, 1, 3)
    final = final.reshape(col_count, seq_count, local_rows, 2, tile_rows).transpose(1, 0, 2, 3, 4)
    chip_sum = exchange_sum(final.reshape(count_rows, 2, tile_rows), "seq")
    result = exchange_sum(chip_sum, "col").astype(jnp.bfloat16)
    return (result[:, 0], result[:, 1])


def solution(mesh):
    return jax.shard_map(
        local,
        mesh=mesh,
        in_specs=(
            P(("col", "seq"), "row"),
            P(("col", "seq"), "row"),
            P("row", ("col", "seq"), None, None, None),
            P("row", ("col", "seq"), None),
            P("row", ("col", "seq")),
            P("row", ("col", "seq"), None, None, None),
            P("row", ("col", "seq"), None),
            P("row", ("col", "seq")),
        ),
        out_specs=(P(("col", "seq"), "row"), P(("col", "seq"), "row")),
        check_vma=False,
    )
```

```python
import jax
import jax.numpy as jnp
from jax import lax
from jax.experimental import pallas as pl
from jax.experimental.pallas import tpu as pltpu
from jax.sharding import PartitionSpec as P

FF = 49152


def gelu_forward(inputs):
    return jax.nn.gelu(inputs, approximate=True)


def gelu_backward(pre_act, gradient):
    return jax.vjp(gelu_forward, pre_act)[1](gradient)[0]


def activate(paired):
    pre_act = paired[0]
    return jnp.stack(
        [
            gelu_forward(pre_act).astype(jnp.bfloat16),
            gelu_backward(pre_act, paired[1]).astype(jnp.bfloat16),
        ]
    )


def group_size(slots):
    best = 1
    for size in range(1, 97):
        if slots % size == 0:
            best = size
    return best


def block_kernel(group, block_cols, pick_row, flips):
    def kernel(codes0, codes1, count0, count1, x, w0, w1, o0, o1):
        step = pl.program_id(0)
        first = step * group

        @pl.when(step == 0)
        def _():
            o0[...] = jnp.zeros_like(o0)
            o1[...] = jnp.zeros_like(o1)

        streams = ((codes0, count0, w0, o0, flips[0], 0), (codes1, count1, w1, o1, flips[1], 1))
        for codes, count, w, o, flipped, which in streams:
            live = count[0, 0]

            @pl.when(first < live)
            def _(codes=codes, w=w, o=o, flipped=flipped, live=live, which=which):
                for j in range(group):
                    slot = first + j
                    code = codes[0, 0, slot]
                    row = lax.div(code, block_cols)
                    col = code - row * block_cols
                    src = x[which, row if pick_row else col]
                    blk = w[j]
                    if flipped:
                        prod = lax.dot_general(
                            src, blk, (((1,), (1,)), ((), ())),
                            preferred_element_type=jnp.float32,
                        )
                    else:
                        prod = jnp.dot(src, blk, preferred_element_type=jnp.float32)
                    scale = jnp.where(slot < live, 1.0, 0.0).astype(jnp.float32)
                    dst = col if pick_row else row
                    o[dst] = o[dst] + prod * scale

    return kernel


def block_pass(x, w0, codes0, count0, w1, codes1, count1, block_cols, pick_row, out_blocks, flips):
    slots, blk, _ = w0.shape
    rows = x.shape[2]
    group = group_size(slots)

    def w_map(which):
        def index_map(i, c0, c1, n0, n1):
            live = (n0, n1)[which][0, 0]
            last = jnp.maximum(live - 1, 0) // group
            return (jnp.minimum(i, last), 0, 0)

        return index_map

    def whole(shape):
        return pl.BlockSpec(shape, lambda i, *refs: (0,) * len(shape))

    spec = pltpu.PrefetchScalarGridSpec(
        num_scalar_prefetch=4,
        grid=(slots // group,),
        in_specs=[
            whole(x.shape),
            pl.BlockSpec((group, blk, blk), w_map(0)),
            pl.BlockSpec((group, blk, blk), w_map(1)),
        ],
        out_specs=[
            whole((out_blocks, rows, blk)),
            whole((out_blocks, rows, blk)),
        ],
    )
    out_shape = [jax.ShapeDtypeStruct((out_blocks, rows, blk), jnp.float32)] * 2
    return pl.pallas_call(
        block_kernel(group, block_cols, pick_row, flips),
        grid_spec=spec,
        out_shape=out_shape,
        compiler_params=pltpu.CompilerParams(dimension_semantics=("arbitrary",)),
    )(codes0, codes1, count0, count1, x, w0, w1)


def exchange_sum(x, axis, wire=jnp.float32, dim=0):
    count = lax.axis_size(axis)
    me = lax.axis_index(axis)
    chunks = x.reshape(x.shape[:dim] + (count, x.shape[dim] // count) + x.shape[dim + 1:])
    total = lax.dynamic_index_in_dim(chunks, me, dim, keepdims=False)
    for shift in range(1, count):
        sent = lax.dynamic_index_in_dim(chunks, (me + shift) % count, dim, keepdims=False)
        sent = sent.astype(wire)
        pairs = [(i, (i + shift) % count) for i in range(count)]
        total = total + lax.ppermute(sent, axis, pairs).astype(jnp.float32)
    return total


def local(tokens, cotangent, up_values, up_index, up_count, down_values, down_index, down_count):
    block_size = up_values.shape[-1]
    tile_rows = tokens.shape[1]
    block_rows = tile_rows // block_size
    block_cols = FF // (block_size * lax.axis_size(("col", "seq")))
    up_vals = up_values[0, 0]
    down_vals = down_values[0, 0]

    stacked = jnp.stack([tokens, cotangent])
    local_rows = stacked.shape[1]
    blocked = stacked.reshape(2, local_rows, block_rows, block_size).transpose(0, 2, 1, 3)
    shard_rows = lax.all_gather(blocked, ("col", "seq"), axis=2, tiled=True)
    pre_part, grad_part = block_pass(
        shard_rows, up_vals, up_index, up_count, down_vals, down_index, down_count,
        block_cols, True, block_cols, (False, True),
    )
    count_rows = pre_part.shape[1]
    pre_flat = pre_part.transpose(1, 0, 2).reshape(count_rows, -1)
    grad_flat = grad_part.transpose(1, 0, 2).reshape(count_rows, -1)
    shares = jnp.stack(
        [exchange_sum(pre_flat, "row"), exchange_sum(grad_flat, "row", jnp.bfloat16)]
    )
    activated = lax.all_gather(activate(shares), "row", axis=1, tiled=True)
    activated = activated.reshape(2, count_rows, block_cols, block_size).transpose(0, 2, 1, 3)
    out_part, back_part = block_pass(
        activated, down_vals, down_index, down_count, up_vals, up_index, up_count,
        block_cols, False, block_rows, (False, True),
    )
    col_count = lax.axis_size("col")
    seq_count = lax.axis_size("seq")
    final = jnp.stack([out_part, back_part]).transpose(0, 2, 1, 3)
    final = final.reshape(2, col_count, seq_count, local_rows, tile_rows).transpose(0, 2, 1, 3, 4)
    chip_sum = exchange_sum(final.reshape(2, count_rows, tile_rows), "seq", dim=1)
    result = exchange_sum(chip_sum, "col", dim=1).astype(jnp.bfloat16)
    return (result[0], result[1])


def solution(mesh):
    return jax.shard_map(
        local,
        mesh=mesh,
        in_specs=(
            P(("col", "seq"), "row"),
            P(("col", "seq"), "row"),
            P("row", ("col", "seq"), None, None, None),
            P("row", ("col", "seq"), None),
            P("row", ("col", "seq")),
            P("row", ("col", "seq"), None, None, None),
            P("row", ("col", "seq"), None),
            P("row", ("col", "seq")),
        ),
        out_specs=(P(("col", "seq"), "row"), P(("col", "seq"), "row")),
        check_vma=False,
    )
```
